32 devices in a mesh: groups: 2 (over y), freq: 4 (over x, core), recv: 4 (over z).
Axes of the slice: x: 2, y: 2, z: 4, core: 2. Of those that a mesh axis runs over, the one named last changes fastest.
Arguments:
- operator: bfloat16 [4, 32, 512, 2048], P('groups', 'freq', 'recv'), parts along dimension 0, may hold values from -0.125 to 0.125
- recorded: float32 [4, 32, 8, 512], P('groups', 'freq', None, 'recv'), parts along dimension 0, may hold values from -18 to 18
- win_start: int32 [16, 16], P('groups'), parts along dimension 0, may hold values from 0 to 15
- win_end: int32 [16, 16], P('groups'), parts along dimension 0, may hold values from 17 to 32
Outputs:
- reflectivity: float32 [4, 32, 8, 2048], P('groups', 'freq', None, 'recv'), parts along dimension 0
- residual: float32 [4, 32, 8, 512], P('groups', 'freq', None, 'recv'), parts along dimension 0
The draws below stay inside these ranges and needn't reach their ends.
There are 2 independent parts, one for each index of `groups`. The reference program is written for one: setup_inputs(seed, part) draws one part's arguments, and reference() takes and returns one part's arrays. A program takes and returns all parts, laid end to end along the dimension named above; each array names one. Nothing has to cross between parts.
All inputs are finite; a program needn't handle non-finite values.
Results may differ from the reference program's by a relative error of at most 0.013.
Values may be sent and summed in bfloat16 or wider, within the bound.
No kernel may reach another device: no remote copies, remote signals or barrier semaphores. Data moves between devices by JAX's collectives and lax.ppermute only.
A program may use at most 64 MiB of HBM per device.

```python
import math
import jax
import jax.numpy as jnp
from jax import lax

F = 32
S = 2048
B = 8
SBLK = 128
ITERS = 5
R = 512
NBLK = 16


def draw_recorded(key, part):
    base_key = jax.random.fold_in(key, 11)
    entry_key, row_key = jax.random.split(base_key, 2)
    entries = jnp.clip(jax.random.normal(entry_key, (2, F, B, R), jnp.float32), -4.0, 4.0)
    ramp_power = 0.5
    row_scale = 0.25 * 10.0 ** jax.random.uniform(row_key, (R,), jnp.float32)
    freq_ids = jnp.arange(F, dtype=jnp.float32)
    freq_scale = 3.0 ** (ramp_power * freq_ids / (F - 1))
    return entries * freq_scale[None, :, None, None] * row_scale[None, None, None, :]


def touch_ends(drawn, stream_key, low, high):
    index_at = [jax.random.randint(jax.random.fold_in(stream_key, axis), (), 0, length) for axis, length in enumerate(drawn.shape)]
    main_axis = drawn.shape.index(max(drawn.shape))
    next_to = index_at[:main_axis] + [(index_at[main_axis] + 1) % drawn.shape[main_axis]] + index_at[main_axis + 1:]
    return drawn.at[tuple(index_at)].set(low).at[tuple(next_to)].set(high)


def shard_levels(key, shape, pieces, low, high):
    gain = 1.0
    for axis_at, blocks in pieces:
        draws = jax.random.uniform(jax.random.fold_in(jax.random.fold_in(key, 6), axis_at), (blocks,), jnp.float32, low / len(pieces), high / len(pieces))
        gain = gain * jnp.repeat(jnp.exp(draws), shape[axis_at] // blocks).reshape((-1,) + (1,) * (len(shape) - 1 - axis_at))
    return gain


def bell_draw(rng, shape, scale, bound, pieces=(), kind=jnp.bfloat16):
    loudness = shard_levels(rng, shape, pieces, -0.22, 0.18) if pieces else 1.0
    values = jax.random.normal(rng, shape, jnp.float32) * scale * loudness
    return jnp.minimum(jnp.maximum(values, -bound), bound).astype(kind)


def setup_inputs(seed: int = 0, part: int = 0) -> dict:
    key_list = jax.random.split(jax.random.key(seed), 5)
    part_keys = jax.random.split(jax.random.fold_in(key_list[4], part), 5)
    operator = bell_draw(part_keys[0], (2, F, R, S), S ** -0.5, 0.125, ((1, 4), (2, 4)))
    recorded = draw_recorded(jax.random.fold_in(jax.random.fold_in(key_list[4], part), 71), part)
    win_start = touch_ends(jax.random.randint(part_keys[2], (B, NBLK), 0, F // 2), jax.random.fold_in(part_keys[2], 1), 0, (F // 2) - 1).astype(jnp.int32)
    win_end = touch_ends(jax.random.randint(part_keys[3], (B, NBLK), F // 2 + 1, F + 1), jax.random.fold_in(part_keys[3], 1), F // 2 + 1, F).astype(jnp.int32)
    return {"operator": operator, "recorded": recorded, "win_start": win_start, "win_end": win_end}


def dft_tables(length):
    positions = jnp.arange(length, dtype=jnp.int32)
    phases = (positions[:, None] * positions[None, :] % length).astype(jnp.float32) * (2.0 * math.pi / length)
    normalizer = 1.0 / math.sqrt(length)
    return (jnp.cos(phases) * normalizer, jnp.sin(phases) * normalizer)

def high_dot(left, right):
    return jnp.dot(left, right, precision=lax.Precision.HIGHEST)

def adjoint(slices):
    res_real, res_imag, op_real, op_imag = slices
    real_part = jnp.dot(res_real, op_real, preferred_element_type=jnp.float32) + jnp.dot(res_imag, op_imag, preferred_element_type=jnp.float32)
    imag_part = jnp.dot(res_imag, op_real, preferred_element_type=jnp.float32) - jnp.dot(res_real, op_imag, preferred_element_type=jnp.float32)
    return jnp.stack([real_part, imag_part])

def forward(slices):
    dir_real, dir_imag, op_real, op_imag = slices
    real_part = jnp.dot(dir_real, op_real.T, preferred_element_type=jnp.float32) - jnp.dot(dir_imag, op_imag.T, preferred_element_type=jnp.float32)
    imag_part = jnp.dot(dir_real, op_imag.T, preferred_element_type=jnp.float32) + jnp.dot(dir_imag, op_real.T, preferred_element_type=jnp.float32)
    return jnp.stack([real_part, imag_part])

def reference(operator, recorded, win_start, win_end):
    cos_table, sin_table = dft_tables(F)
    block_ids = jnp.arange(S, dtype=jnp.int32) // SBLK
    opening = win_start[:, block_ids].reshape(-1)
    closing = win_end[:, block_ids].reshape(-1)
    samples = jnp.arange(F, dtype=jnp.int32)[:, None]
    window = ((samples >= opening[None, :]) & (samples < closing[None, :])).astype(jnp.float32)
    reflect = jnp.zeros((2, F, B, S), jnp.float32)
    residual = recorded
    for iteration in range(ITERS):
        rounded_residual = residual.astype(jnp.bfloat16)
        gradient = lax.map(adjoint, (rounded_residual[0], rounded_residual[1], operator[0], operator[1]))
        gradient = jnp.moveaxis(gradient, 1, 0).reshape(2, F, B * S)
        time_real = high_dot(cos_table.T, gradient[0]) - high_dot(sin_table.T, gradient[1])
        time_imag = high_dot(sin_table.T, gradient[0]) + high_dot(cos_table.T, gradient[1])
        kept_real = time_real * window
        kept_imag = time_imag * window
        dir_real = high_dot(cos_table, kept_real) + high_dot(sin_table, kept_imag)
        dir_imag = high_dot(cos_table, kept_imag) - high_dot(sin_table, kept_real)
        direction = jnp.stack([dir_real, dir_imag]).reshape(2, F, B, S)
        rounded_direction = direction.astype(jnp.bfloat16)
        image = lax.map(forward, (rounded_direction[0], rounded_direction[1], operator[0], operator[1]))
        image = jnp.moveaxis(image, 1, 0)
        step_length = jnp.sum(direction * direction) / (jnp.sum(image * image) + 1e-06)
        reflect = reflect + step_length * direction
        residual = residual - step_length * image
    return (reflect, residual)
```

```python
import math

import jax
import jax.numpy as jnp
from jax import lax
from jax.sharding import PartitionSpec as P

SBLK = 128
LINK_TYPE = jnp.float32
ITERS = 5


def high_dot(left, right):
    return jnp.dot(left, right, precision=lax.Precision.HIGHEST)


def dft_rows(row_ids, length):
    positions = jnp.arange(length, dtype=jnp.int32)
    phases = (row_ids[:, None] * positions[None, :] % length).astype(jnp.float32) * (
        2.0 * math.pi / length
    )
    normalizer = 1.0 / math.sqrt(length)
    return (jnp.cos(phases) * normalizer, jnp.sin(phases) * normalizer)


def window_mask(column_ids, src_local, win_start, win_end, length):
    blocks = win_start.shape[1]
    side_ids = column_ids // src_local
    source_ids = lax.axis_index("recv") * src_local + column_ids % src_local
    flat_ids = side_ids * blocks + source_ids // SBLK
    table_ids = jnp.arange(win_start.shape[0] * blocks, dtype=jnp.int32)
    matches = flat_ids[:, None] == table_ids[None, :]
    opening = jnp.sum(jnp.where(matches, win_start.reshape(-1)[None, :], 0), axis=1)
    closing = jnp.sum(jnp.where(matches, win_end.reshape(-1)[None, :], 0), axis=1)
    samples = jnp.arange(length, dtype=jnp.int32)[:, None]
    return ((samples >= opening[None, :]) & (samples < closing[None, :])).astype(jnp.float32)


def adjoint(res, real_operator, imag_operator):
    real_part = jnp.einsum(
        "fbr,frs->fbs", res[0], real_operator, preferred_element_type=jnp.float32
    ) + jnp.einsum("fbr,frs->fbs", res[1], imag_operator, preferred_element_type=jnp.float32)
    imag_part = jnp.einsum(
        "fbr,frs->fbs", res[1], real_operator, preferred_element_type=jnp.float32
    ) - jnp.einsum("fbr,frs->fbs", res[0], imag_operator, preferred_element_type=jnp.float32)
    return jnp.stack([real_part, imag_part])


def split_adjoint(values, real_operator, imag_operator):
    high, low = split_high_low(values)
    doubled = adjoint(jnp.concatenate([high, low], axis=2), real_operator, imag_operator)
    rows = values.shape[2]
    return doubled[:, :, :rows] + doubled[:, :, rows:]


def forward(direction, real_operator, imag_operator):
    real_part = jnp.einsum(
        "fbs,frs->fbr", direction[0], real_operator, preferred_element_type=jnp.float32
    ) - jnp.einsum("fbs,frs->fbr", direction[1], imag_operator, preferred_element_type=jnp.float32)
    imag_part = jnp.einsum(
        "fbs,frs->fbr", direction[0], imag_operator, preferred_element_type=jnp.float32
    ) + jnp.einsum("fbs,frs->fbr", direction[1], real_operator, preferred_element_type=jnp.float32)
    return jnp.stack([real_part, imag_part])


def split_high_low(values):
    high = lax.reduce_precision(values, exponent_bits=8, mantissa_bits=7)
    return high.astype(jnp.bfloat16), (values - high).astype(jnp.bfloat16)


def split_parts(values):
    pieces = []
    for value in values:
        high = lax.reduce_precision(value, exponent_bits=8, mantissa_bits=7)
        rest = value - high
        middle = lax.reduce_precision(rest, exponent_bits=8, mantissa_bits=7)
        pieces += [high, middle, rest - middle]
    return jnp.stack(pieces)


def reduce_gather(partial):
    scattered = lax.psum_scatter(
        partial.astype(LINK_TYPE), "recv", scatter_dimension=3, tiled=True
    )
    flat = scattered.reshape(scattered.shape[0], scattered.shape[1], -1)
    return lax.all_gather(flat, "freq", axis=1, tiled=True).astype(jnp.float32)


def gather_sources(block, values):
    src_local = block.shape[-1]
    recv_size = lax.axis_size("recv")
    rows = jnp.concatenate(split_high_low(block.reshape(-1, src_local)))
    pieces = split_parts(values)
    extra = jnp.zeros((16, src_local), jnp.float32).at[0, : pieces.shape[0]].set(pieces)
    payload = jnp.concatenate([rows, extra.astype(jnp.bfloat16)])
    gathered = lax.all_gather(payload, "recv", axis=1, tiled=True)
    count = rows.shape[0]
    half = count // 2
    joined = gathered[:half].astype(jnp.float32) + gathered[half:count].astype(jnp.float32)
    full = joined.reshape(block.shape[:-1] + (recv_size * src_local,))
    tail = gathered[count].reshape(recv_size, src_local)[:, : pieces.shape[0]].astype(jnp.float32)
    sums = jnp.sum(tail.reshape(recv_size, len(values), 3), axis=(0, 2))
    return full, sums


def on_device(operator, recorded, win_start, win_end):
    freq_local = operator.shape[1]
    sources = operator.shape[3]
    right_sides = recorded.shape[2]
    src_local = sources // lax.axis_size("recv")
    total_freq = freq_local * lax.axis_size("freq")
    columns = right_sides * src_local
    real_operator = operator[0]
    imag_operator = operator[1]

    cos_all, sin_all = dft_rows(jnp.arange(total_freq, dtype=jnp.int32), total_freq)
    own_rows = lax.axis_index("freq") * freq_local + jnp.arange(freq_local, dtype=jnp.int32)
    cos_own, sin_own = dft_rows(own_rows, total_freq)
    window = window_mask(
        jnp.arange(columns, dtype=jnp.int32), src_local, win_start, win_end, total_freq
    )
    block_shape = (2, freq_local, right_sides, src_local)

    def to_time(spectrum):
        time_real = high_dot(cos_all.T, spectrum[0]) - high_dot(sin_all.T, spectrum[1])
        time_imag = high_dot(sin_all.T, spectrum[0]) + high_dot(cos_all.T, spectrum[1])
        return time_real, time_imag

    def to_own_freq(kept_real, kept_imag):
        real_part = high_dot(cos_own, kept_real) + high_dot(sin_own, kept_imag)
        imag_part = high_dot(cos_own, kept_imag) - high_dot(sin_own, kept_real)
        return jnp.stack([real_part, imag_part]).reshape(block_shape)

    gradient = reduce_gather(split_adjoint(recorded, real_operator, imag_operator))
    time_real, time_imag = to_time(gradient)
    kept_real = time_real * window
    kept_imag = time_imag * window
    kept_power = jnp.sum(kept_real * kept_real + kept_imag * kept_imag)
    direction_own = to_own_freq(kept_real, kept_imag)
    direction_all, sums = gather_sources(direction_own, [kept_power])
    direction_power = sums[0]

    reflect = jnp.zeros(block_shape, jnp.float32)
    residual = recorded
    for iteration in range(ITERS):
        image = forward(direction_all.astype(jnp.bfloat16), real_operator, imag_operator)
        if iteration < ITERS - 1:
            normal = reduce_gather(split_adjoint(image, real_operator, imag_operator))
            normal_real, normal_imag = to_time(normal)
            image_part = jnp.sum(kept_real * normal_real + kept_imag * normal_imag)
            masked_real = normal_real * window
            masked_imag = normal_imag * window
            change_own = to_own_freq(masked_real, masked_imag)
            values = [image_part] if iteration == 0 else [image_part, kept_power]
            change_all, sums = gather_sources(change_own, values)
            image_energy = sums[0]
            if iteration > 0:
                direction_power = sums[1]
            step_length = direction_power / (image_energy + 1e-06)
            reflect = reflect + step_length * direction_own
            residual = residual - step_length * image
            direction_all = direction_all - step_length * change_all
            direction_own = direction_own - step_length * change_own
            kept_real = kept_real - step_length * masked_real
            kept_imag = kept_imag - step_length * masked_imag
            kept_power = jnp.sum(kept_real * kept_real + kept_imag * kept_imag)
        else:
            own_power = jnp.where(lax.axis_index("freq") == 0, kept_power, 0.0)
            direction_power, image_energy = lax.psum(
                (own_power, jnp.sum(image * image)), ("freq", "recv")
            )
            step_length = direction_power / (image_energy + 1e-06)
            reflect = reflect + step_length * direction_own
            residual = residual - step_length * image
    return (reflect, residual)


def solution(mesh):
    return jax.shard_map(
        on_device,
        mesh=mesh,
        in_specs=(
            P("groups", "freq", "recv", None),
            P("groups", "freq", None, "recv"),
            P("groups", None),
            P("groups", None),
        ),
        out_specs=(P("groups", "freq", None, "recv"), P("groups", "freq", None, "recv")),
        check_vma=False,
    )
```

```python
import math

import jax
import jax.numpy as jnp
from jax import lax
from jax.sharding import PartitionSpec as P

SBLK = 128
ITERS = 5


def high_dot(left, right):
    return jnp.dot(left, right, precision=lax.Precision.HIGHEST)


def dft_rows(row_ids, length):
    positions = jnp.arange(length, dtype=jnp.int32)
    phases = (row_ids[:, None] * positions[None, :] % length).astype(jnp.float32) * (
        2.0 * math.pi / length
    )
    normalizer = 1.0 / math.sqrt(length)
    return (jnp.cos(phases) * normalizer, jnp.sin(phases) * normalizer)


def to_time(real_part, imag_part, cos_rows, sin_rows):
    time_real = high_dot(cos_rows.T, real_part) - high_dot(sin_rows.T, imag_part)
    time_imag = high_dot(sin_rows.T, real_part) + high_dot(cos_rows.T, imag_part)
    return (time_real, time_imag)


def to_freq(kept_real, kept_imag, cos_rows, sin_rows):
    real_part = high_dot(cos_rows, kept_real) + high_dot(sin_rows, kept_imag)
    imag_part = high_dot(cos_rows, kept_imag) - high_dot(sin_rows, kept_real)
    return jnp.stack([real_part, imag_part])


def window_mask(column_ids, src_local, win_start, win_end, length):
    blocks = win_start.shape[1]
    side_ids = column_ids // src_local
    source_ids = lax.axis_index("recv") * src_local + column_ids % src_local
    flat_ids = side_ids * blocks + source_ids // SBLK
    table_ids = jnp.arange(win_start.shape[0] * blocks, dtype=jnp.int32)
    matches = flat_ids[:, None] == table_ids[None, :]
    opening = jnp.sum(jnp.where(matches, win_start.reshape(-1)[None, :], 0), axis=1)
    closing = jnp.sum(jnp.where(matches, win_end.reshape(-1)[None, :], 0), axis=1)
    samples = jnp.arange(length, dtype=jnp.int32)[:, None]
    return ((samples >= opening[None, :]) & (samples < closing[None, :])).astype(jnp.float32)


def on_device(operator, recorded, win_start, win_end):
    freq_local = operator.shape[1]
    sources = operator.shape[3]
    right_sides = recorded.shape[2]
    src_local = sources // lax.axis_size("recv")
    total_freq = freq_local * lax.axis_size("freq")
    columns = right_sides * src_local
    real_operator = operator[0]
    imag_operator = operator[1]
    reflect = jnp.zeros((2, freq_local, right_sides, src_local), jnp.float32)
    residual = recorded
    for iteration in range(ITERS):
        rounded_residual = residual.astype(jnp.bfloat16)
        stacked_residual = jnp.concatenate([rounded_residual[0], rounded_residual[1]], axis=1)
        with_real = jnp.einsum(
            "fbr,frs->fbs", stacked_residual, real_operator, preferred_element_type=jnp.float32
        )
        with_imag = jnp.einsum(
            "fbr,frs->fbs", stacked_residual, imag_operator, preferred_element_type=jnp.float32
        )
        partial_real = with_real[:, :right_sides] + with_imag[:, right_sides:]
        partial_imag = with_real[:, right_sides:] - with_imag[:, :right_sides]
        gradient = lax.psum_scatter(
            jnp.stack([partial_real, partial_imag]).astype(jnp.bfloat16),
            "recv",
            scatter_dimension=3,
            tiled=True,
        ).astype(jnp.float32)
        flattened = gradient.reshape(2, freq_local, columns)
        empty_time = jnp.zeros((2, total_freq, columns), jnp.float32)
        segment = lax.all_gather(flattened.astype(jnp.bfloat16), "freq", axis=1, tiled=True).astype(
            jnp.float32
        )
        row_ids = jnp.arange(segment.shape[1], dtype=jnp.int32)
        cos_part, sin_part = dft_rows(row_ids, total_freq)
        part_real, part_imag = to_time(segment[0], segment[1], cos_part, sin_part)
        timed = empty_time + jnp.stack([part_real, part_imag])
        window = window_mask(
            jnp.arange(columns, dtype=jnp.int32), src_local, win_start, win_end, total_freq
        )
        own_rows = lax.axis_index("freq") * freq_local + jnp.arange(freq_local, dtype=jnp.int32)
        cos_rows, sin_rows = dft_rows(own_rows, total_freq)
        projected = to_freq(timed[0] * window, timed[1] * window, cos_rows, sin_rows)
        direction = projected.reshape(2, freq_local, right_sides, src_local)
        rounded_direction = direction.astype(jnp.bfloat16)
        add_segment = lax.all_gather(rounded_direction, "recv", axis=3, tiled=True)
        stacked_direction = jnp.concatenate([add_segment[0], add_segment[1]], axis=1)
        by_real = jnp.einsum(
            "fbs,frs->fbr", stacked_direction, real_operator, preferred_element_type=jnp.float32
        )
        by_imag = jnp.einsum(
            "fbs,frs->fbr", stacked_direction, imag_operator, preferred_element_type=jnp.float32
        )
        image_real = by_real[:, :right_sides] - by_imag[:, right_sides:]
        image_imag = by_imag[:, :right_sides] + by_real[:, right_sides:]
        image = jnp.stack([image_real, image_imag])
        direction_power, image_energy = lax.psum(
            lax.psum((jnp.sum(direction * direction), jnp.sum(image * image)), "recv"), "freq"
        )
        step_length = direction_power / (image_energy + 1e-06)
        reflect = reflect + step_length * direction
        residual = residual - step_length * image
    return (reflect, residual)


def solution(mesh):
    return jax.shard_map(
        on_device,
        mesh=mesh,
        in_specs=(
            P("groups", "freq", "recv", None),
            P("groups", "freq", None, "recv"),
            P("groups", None),
            P("groups", None),
        ),
        out_specs=(P("groups", "freq", None, "recv"), P("groups", "freq", None, "recv")),
        check_vma=False,
    )
```

```python
import math

import jax
import jax.numpy as jnp
from jax import lax
from jax.sharding import PartitionSpec as P

SBLK = 128
ITERS = 5


def high_dot(left, right):
    return jnp.dot(left, right, precision=lax.Precision.HIGHEST)


def dft_rows(row_ids, length):
    positions = jnp.arange(length, dtype=jnp.int32)
    phases = (row_ids[:, None] * positions[None, :] % length).astype(jnp.float32) * (
        2.0 * math.pi / length
    )
    normalizer = 1.0 / math.sqrt(length)
    return (jnp.cos(phases) * normalizer, jnp.sin(phases) * normalizer)


def window_mask(column_ids, src_local, win_start, win_end, length):
    blocks = win_start.shape[1]
    side_ids = column_ids // src_local
    source_ids = lax.axis_index("recv") * src_local + column_ids % src_local
    flat_ids = side_ids * blocks + source_ids // SBLK
    table_ids = jnp.arange(win_start.shape[0] * blocks, dtype=jnp.int32)
    matches = flat_ids[:, None] == table_ids[None, :]
    opening = jnp.sum(jnp.where(matches, win_start.reshape(-1)[None, :], 0), axis=1)
    closing = jnp.sum(jnp.where(matches, win_end.reshape(-1)[None, :], 0), axis=1)
    samples = jnp.arange(length, dtype=jnp.int32)[:, None]
    return ((samples >= opening[None, :]) & (samples < closing[None, :])).astype(jnp.float32)


def on_device(operator, recorded, win_start, win_end):
    freq_local = operator.shape[1]
    sources = operator.shape[3]
    right_sides = recorded.shape[2]
    src_local = sources // lax.axis_size("recv")
    total_freq = freq_local * lax.axis_size("freq")
    columns = right_sides * src_local
    real_operator = operator[0]
    imag_operator = operator[1]

    cos_part, sin_part = dft_rows(jnp.arange(total_freq, dtype=jnp.int32), total_freq)
    to_time = jnp.block([[cos_part.T, -sin_part.T], [sin_part.T, cos_part.T]])
    own_rows = lax.axis_index("freq") * freq_local + jnp.arange(freq_local, dtype=jnp.int32)
    cos_rows, sin_rows = dft_rows(own_rows, total_freq)
    to_freq = jnp.block([[cos_rows, sin_rows], [-sin_rows, cos_rows]])
    window = window_mask(
        jnp.arange(columns, dtype=jnp.int32), src_local, win_start, win_end, total_freq
    )
    window = jnp.concatenate([window, window])

    def step(iteration, state):
        reflect, residual = state
        rounded_residual = residual.astype(jnp.bfloat16)
        stacked_residual = jnp.concatenate([rounded_residual[0], rounded_residual[1]], axis=1)
        with_real = jnp.einsum(
            "fbr,frs->fbs", stacked_residual, real_operator, preferred_element_type=jnp.float32
        )
        with_imag = jnp.einsum(
            "fbr,frs->fbs", stacked_residual, imag_operator, preferred_element_type=jnp.float32
        )
        partial_real = with_real[:, :right_sides] + with_imag[:, right_sides:]
        partial_imag = with_real[:, right_sides:] - with_imag[:, :right_sides]
        gradient = lax.psum_scatter(
            jnp.stack([partial_real, partial_imag]).astype(jnp.bfloat16),
            "recv",
            scatter_dimension=3,
            tiled=True,
        )
        flattened = gradient.reshape(2, freq_local, columns)
        segment = lax.all_gather(flattened, "freq", axis=1, tiled=True).astype(jnp.float32)
        timed = high_dot(to_time, segment.reshape(2 * total_freq, columns))
        projected = high_dot(to_freq, timed * window)
        direction = projected.reshape(2, freq_local, right_sides, src_local)
        rounded_direction = direction.astype(jnp.bfloat16)
        add_segment = lax.all_gather(rounded_direction, "recv", axis=3, tiled=True)
        stacked_direction = jnp.concatenate([add_segment[0], add_segment[1]], axis=1)
        by_real = jnp.einsum(
            "fbs,frs->fbr", stacked_direction, real_operator, preferred_element_type=jnp.float32
        )
        by_imag = jnp.einsum(
            "fbs,frs->fbr", stacked_direction, imag_operator, preferred_element_type=jnp.float32
        )
        image_real = by_real[:, :right_sides] - by_imag[:, right_sides:]
        image_imag = by_imag[:, :right_sides] + by_real[:, right_sides:]
        image = jnp.stack([image_real, image_imag])
        direction_power, image_energy = lax.psum(
            lax.psum((jnp.sum(direction * direction), jnp.sum(image * image)), "recv"), "freq"
        )
        step_length = direction_power / (image_energy + 1e-06)
        return (reflect + step_length * direction, residual - step_length * image)

    reflect = jnp.zeros((2, freq_local, right_sides, src_local), jnp.float32)
    return lax.fori_loop(0, ITERS, step, (reflect, recorded))


def solution(mesh):
    return jax.shard_map(
        on_device,
        mesh=mesh,
        in_specs=(
            P("groups", "freq", "recv", None),
            P("groups", "freq", None, "recv"),
            P("groups", None),
            P("groups", None),
        ),
        out_specs=(P("groups", "freq", None, "recv"), P("groups", "freq", None, "recv")),
        check_vma=False,
    )
```

```python
import math

import jax
import jax.numpy as jnp
from jax import lax
from jax.sharding import PartitionSpec as P

SBLK = 128
ITERS = 5


def high_dot(left, right):
    return jnp.dot(left, right, precision=lax.Precision.HIGHEST)


def dft_rows(row_ids, length):
    positions = jnp.arange(length, dtype=jnp.int32)
    phases = (row_ids[:, None] * positions[None, :] % length).astype(jnp.float32) * (
        2.0 * math.pi / length
    )
    normalizer = 1.0 / math.sqrt(length)
    return (jnp.cos(phases) * normalizer, jnp.sin(phases) * normalizer)


def window_mask(column_ids, src_local, win_start, win_end, length):
    blocks = win_start.shape[1]
    side_ids = column_ids // src_local
    source_ids = lax.axis_index("recv") * src_local + column_ids % src_local
    flat_ids = side_ids * blocks + source_ids // SBLK
    table_ids = jnp.arange(win_start.shape[0] * blocks, dtype=jnp.int32)
    matches = flat_ids[:, None] == table_ids[None, :]
    opening = jnp.sum(jnp.where(matches, win_start.reshape(-1)[None, :], 0), axis=1)
    closing = jnp.sum(jnp.where(matches, win_end.reshape(-1)[None, :], 0), axis=1)
    samples = jnp.arange(length, dtype=jnp.int32)[:, None]
    return ((samples >= opening[None, :]) & (samples < closing[None, :])).astype(jnp.float32)


def shifted(value, axis, distance):
    size = lax.axis_size(axis)
    return lax.ppermute(value, axis, [(i, (i + distance) % size) for i in range(size)])


def sum_scatter(partial, axis, dim):
    size = lax.axis_size(axis)
    me = lax.axis_index(axis)
    blocks = partial.reshape(partial.shape[:dim] + (size, partial.shape[dim] // size) + partial.shape[dim + 1 :])
    total = lax.dynamic_index_in_dim(blocks, me, axis=dim, keepdims=False).astype(jnp.float32)
    for distance in range(1, size):
        piece = lax.dynamic_index_in_dim(blocks, (me + distance) % size, axis=dim, keepdims=False)
        total = total + shifted(piece, axis, distance).astype(jnp.float32)
    return total


def gather_blocks(block, axis, dim):
    size = lax.axis_size(axis)
    me = lax.axis_index(axis)
    slots = jnp.stack([block] + [shifted(block, axis, d) for d in range(1, size)], axis=dim)
    order = (me - jnp.arange(size, dtype=jnp.int32)) % size
    ordered = jnp.take(slots, order, axis=dim)
    return ordered.reshape(block.shape[:dim] + (size * block.shape[dim],) + block.shape[dim + 1 :])


def on_device(operator, recorded, win_start, win_end):
    freq_local = operator.shape[1]
    sources = operator.shape[3]
    right_sides = recorded.shape[2]
    src_local = sources // lax.axis_size("recv")
    total_freq = freq_local * lax.axis_size("freq")
    columns = right_sides * src_local
    real_operator = operator[0]
    imag_operator = operator[1]

    cos_part, sin_part = dft_rows(jnp.arange(total_freq, dtype=jnp.int32), total_freq)
    to_time = jnp.block([[cos_part.T, -sin_part.T], [sin_part.T, cos_part.T]])
    own_rows = lax.axis_index("freq") * freq_local + jnp.arange(freq_local, dtype=jnp.int32)
    cos_rows, sin_rows = dft_rows(own_rows, total_freq)
    to_freq = jnp.block([[cos_rows, sin_rows], [-sin_rows, cos_rows]])
    window = window_mask(
        jnp.arange(columns, dtype=jnp.int32), src_local, win_start, win_end, total_freq
    )
    window = jnp.concatenate([window, window])

    def step(iteration, state):
        reflect, residual = state
        rounded_residual = residual.astype(jnp.bfloat16)
        stacked_residual = jnp.concatenate([rounded_residual[0], rounded_residual[1]], axis=1)
        with_real = jnp.einsum(
            "fbr,frs->fbs", stacked_residual, real_operator, preferred_element_type=jnp.float32
        )
        with_imag = jnp.einsum(
            "fbr,frs->fbs", stacked_residual, imag_operator, preferred_element_type=jnp.float32
        )
        partial_real = with_real[:, :right_sides] + with_imag[:, right_sides:]
        partial_imag = with_real[:, right_sides:] - with_imag[:, :right_sides]
        gradient = sum_scatter(
            jnp.stack([partial_real, partial_imag]).astype(jnp.bfloat16), "recv", 3
        )
        flattened = gradient.astype(jnp.bfloat16).reshape(2, freq_local, columns)
        segment = gather_blocks(flattened, "freq", 1).astype(jnp.float32)
        timed = high_dot(to_time, segment.reshape(2 * total_freq, columns))
        projected = high_dot(to_freq, timed * window)
        direction = projected.reshape(2, freq_local, right_sides, src_local)
        rounded_direction = direction.astype(jnp.bfloat16)
        add_segment = gather_blocks(rounded_direction, "recv", 3)
        stacked_direction = jnp.concatenate([add_segment[0], add_segment[1]], axis=1)
        by_real = jnp.einsum(
            "fbs,frs->fbr", stacked_direction, real_operator, preferred_element_type=jnp.float32
        )
        by_imag = jnp.einsum(
            "fbs,frs->fbr", stacked_direction, imag_operator, preferred_element_type=jnp.float32
        )
        image_real = by_real[:, :right_sides] - by_imag[:, right_sides:]
        image_imag = by_imag[:, :right_sides] + by_real[:, right_sides:]
        image = jnp.stack([image_real, image_imag])
        direction_power, image_energy = lax.psum(
            lax.psum((jnp.sum(direction * direction), jnp.sum(image * image)), "recv"), "freq"
        )
        step_length = direction_power / (image_energy + 1e-06)
        return (reflect + step_length * direction, residual - step_length * image)

    reflect = jnp.zeros((2, freq_local, right_sides, src_local), jnp.float32)
    return lax.fori_loop(0, ITERS, step, (reflect, recorded))


def solution(mesh):
    return jax.shard_map(
        on_device,
        mesh=mesh,
        in_specs=(
            P("groups", "freq", "recv", None),
            P("groups", "freq", None, "recv"),
            P("groups", None),
            P("groups", None),
        ),
        out_specs=(P("groups", "freq", None, "recv"), P("groups", "freq", None, "recv")),
        check_vma=False,
    )
```

```python
import math

import jax
import jax.numpy as jnp
from jax import lax
from jax.sharding import PartitionSpec as P

SBLK = 128
ITERS = 5


def high_dot(left, right):
    return jnp.dot(left, right, precision=lax.Precision.HIGHEST)


def dft_rows(row_ids, length):
    positions = jnp.arange(length, dtype=jnp.int32)
    phases = (row_ids[:, None] * positions[None, :] % length).astype(jnp.float32) * (
        2.0 * math.pi / length
    )
    normalizer = 1.0 / math.sqrt(length)
    return (jnp.cos(phases) * normalizer, jnp.sin(phases) * normalizer)


def window_mask(column_ids, src_local, win_start, win_end, length):
    blocks = win_start.shape[1]
    side_ids = column_ids // src_local
    source_ids = lax.axis_index("recv") * src_local + column_ids % src_local
    flat_ids = side_ids * blocks + source_ids // SBLK
    table_ids = jnp.arange(win_start.shape[0] * blocks, dtype=jnp.int32)
    matches = flat_ids[:, None] == table_ids[None, :]
    opening = jnp.sum(jnp.where(matches, win_start.reshape(-1)[None, :], 0), axis=1)
    closing = jnp.sum(jnp.where(matches, win_end.reshape(-1)[None, :], 0), axis=1)
    samples = jnp.arange(length, dtype=jnp.int32)[:, None]
    return ((samples >= opening[None, :]) & (samples < closing[None, :])).astype(jnp.float32)


def shifted(value, axis, distance):
    size = lax.axis_size(axis)
    return lax.ppermute(value, axis, [(i, (i + distance) % size) for i in range(size)])


def sum_scatter(partial, axis, dim):
    size = lax.axis_size(axis)
    me = lax.axis_index(axis)
    blocks = partial.reshape(partial.shape[:dim] + (size, partial.shape[dim] // size) + partial.shape[dim + 1 :])
    total = lax.dynamic_index_in_dim(blocks, me, axis=dim, keepdims=False).astype(jnp.float32)
    for distance in range(1, size):
        piece = lax.dynamic_index_in_dim(blocks, (me + distance) % size, axis=dim, keepdims=False)
        total = total + shifted(piece, axis, distance).astype(jnp.float32)
    return total


def gather_blocks(block, axis, dim):
    size = lax.axis_size(axis)
    me = lax.axis_index(axis)
    slots = jnp.stack([block] + [shifted(block, axis, d) for d in range(1, size)], axis=dim)
    order = (me - jnp.arange(size, dtype=jnp.int32)) % size
    ordered = jnp.take(slots, order, axis=dim)
    return ordered.reshape(block.shape[:dim] + (size * block.shape[dim],) + block.shape[dim + 1 :])


def on_device(operator, recorded, win_start, win_end):
    freq_local = operator.shape[1]
    sources = operator.shape[3]
    right_sides = recorded.shape[2]
    src_local = sources // lax.axis_size("recv")
    total_freq = freq_local * lax.axis_size("freq")
    columns = right_sides * src_local
    real_operator = operator[0]
    imag_operator = operator[1]

    cos_part, sin_part = dft_rows(jnp.arange(total_freq, dtype=jnp.int32), total_freq)
    to_time = jnp.block([[cos_part.T, -sin_part.T], [sin_part.T, cos_part.T]])
    own_rows = lax.axis_index("freq") * freq_local + jnp.arange(freq_local, dtype=jnp.int32)
    cos_rows, sin_rows = dft_rows(own_rows, total_freq)
    to_freq = jnp.block([[cos_rows, sin_rows], [-sin_rows, cos_rows]])
    window = window_mask(
        jnp.arange(columns, dtype=jnp.int32), src_local, win_start, win_end, total_freq
    )
    window = jnp.concatenate([window, window])

    def step(iteration, state):
        reflect, residual = state
        rounded_residual = residual.astype(jnp.bfloat16)
        stacked_residual = jnp.concatenate([rounded_residual[0], rounded_residual[1]], axis=1)
        with_real = jnp.einsum(
            "fbr,frs->fbs", stacked_residual, real_operator, preferred_element_type=jnp.float32
        )
        with_imag = jnp.einsum(
            "fbr,frs->fbs", stacked_residual, imag_operator, preferred_element_type=jnp.float32
        )
        partial_real = with_real[:, :right_sides] + with_imag[:, right_sides:]
        partial_imag = with_real[:, right_sides:] - with_imag[:, :right_sides]
        gradient = sum_scatter(
            jnp.stack([partial_real, partial_imag]).astype(jnp.bfloat16), "recv", 3
        )
        flattened = gradient.astype(jnp.bfloat16).reshape(2, freq_local, columns)
        segment = lax.all_gather(flattened, "freq", axis=1, tiled=True).astype(jnp.float32)
        timed = high_dot(to_time, segment.reshape(2 * total_freq, columns))
        projected = high_dot(to_freq, timed * window)
        direction = projected.reshape(2, freq_local, right_sides, src_local)
        rounded_direction = direction.astype(jnp.bfloat16)
        add_segment = gather_blocks(rounded_direction, "recv", 3)
        stacked_direction = jnp.concatenate([add_segment[0], add_segment[1]], axis=1)
        by_real = jnp.einsum(
            "fbs,frs->fbr", stacked_direction, real_operator, preferred_element_type=jnp.float32
        )
        by_imag = jnp.einsum(
            "fbs,frs->fbr", stacked_direction, imag_operator, preferred_element_type=jnp.float32
        )
        image_real = by_real[:, :right_sides] - by_imag[:, right_sides:]
        image_imag = by_imag[:, :right_sides] + by_real[:, right_sides:]
        image = jnp.stack([image_real, image_imag])
        sums = jnp.stack([jnp.sum(direction * direction), jnp.sum(image * image)])
        sums = jnp.sum(gather_blocks(sums[None], "recv", 0), axis=0)
        direction_power, image_energy = jnp.sum(gather_blocks(sums[None], "freq", 0), axis=0)
        step_length = direction_power / (image_energy + 1e-06)
        return (reflect + step_length * direction, residual - step_length * image)

    reflect = jnp.zeros((2, freq_local, right_sides, src_local), jnp.float32)
    return lax.fori_loop(0, ITERS, step, (reflect, recorded))


def solution(mesh):
    return jax.shard_map(
        on_device,
        mesh=mesh,
        in_specs=(
            P("groups", "freq", "recv", None),
            P("groups", "freq", None, "recv"),
            P("groups", None),
            P("groups", None),
        ),
        out_specs=(P("groups", "freq", None, "recv"), P("groups", "freq", None, "recv")),
        check_vma=False,
    )
```

```python
import math

import jax
import jax.numpy as jnp
from jax import lax
from jax.experimental import pallas as pl
from jax.experimental.pallas import tpu as pltpu
from jax.sharding import PartitionSpec as P

SBLK = 128
ITERS = 5


def high_dot(left, right):
    return jnp.dot(left, right, precision=lax.Precision.HIGHEST)


def dft_rows(row_ids, length):
    positions = jnp.arange(length, dtype=jnp.int32)
    phases = (row_ids[:, None] * positions[None, :] % length).astype(jnp.float32) * (
        2.0 * math.pi / length
    )
    normalizer = 1.0 / math.sqrt(length)
    return (jnp.cos(phases) * normalizer, jnp.sin(phases) * normalizer)


def window_mask(column_ids, src_local, win_start, win_end, length):
    blocks = win_start.shape[1]
    side_ids = column_ids // src_local
    source_ids = lax.axis_index("recv") * src_local + column_ids % src_local
    flat_ids = side_ids * blocks + source_ids // SBLK
    table_ids = jnp.arange(win_start.shape[0] * blocks, dtype=jnp.int32)
    matches = flat_ids[:, None] == table_ids[None, :]
    opening = jnp.sum(jnp.where(matches, win_start.reshape(-1)[None, :], 0), axis=1)
    closing = jnp.sum(jnp.where(matches, win_end.reshape(-1)[None, :], 0), axis=1)
    samples = jnp.arange(length, dtype=jnp.int32)[:, None]
    return ((samples >= opening[None, :]) & (samples < closing[None, :])).astype(jnp.float32)


def shifted(value, axis, distance):
    size = lax.axis_size(axis)
    return lax.ppermute(value, axis, [(i, (i + distance) % size) for i in range(size)])


def sum_scatter(partial, axis, dim):
    size = lax.axis_size(axis)
    me = lax.axis_index(axis)
    blocks = partial.reshape(partial.shape[:dim] + (size, partial.shape[dim] // size) + partial.shape[dim + 1 :])
    total = lax.dynamic_index_in_dim(blocks, me, axis=dim, keepdims=False).astype(jnp.float32)
    for distance in range(1, size):
        piece = lax.dynamic_index_in_dim(blocks, (me + distance) % size, axis=dim, keepdims=False)
        total = total + shifted(piece, axis, distance).astype(jnp.float32)
    return total


def gather_blocks(block, axis, dim):
    size = lax.axis_size(axis)
    me = lax.axis_index(axis)
    slots = jnp.stack([block] + [shifted(block, axis, d) for d in range(1, size)], axis=dim)
    order = (me - jnp.arange(size, dtype=jnp.int32)) % size
    ordered = jnp.take(slots, order, axis=dim)
    return ordered.reshape(block.shape[:dim] + (size * block.shape[dim],) + block.shape[dim + 1 :])


def adjoint_kernel(res_ref, op_ref, out_ref):
    rows = out_ref.shape[2]
    res = res_ref[0]
    by_real = jnp.dot(res, op_ref[0, 0], preferred_element_type=jnp.float32)
    by_imag = jnp.dot(res, op_ref[1, 0], preferred_element_type=jnp.float32)
    out_ref[0, 0] = (by_real[:rows] + by_imag[rows:]).astype(out_ref.dtype)
    out_ref[1, 0] = (by_real[rows:] - by_imag[:rows]).astype(out_ref.dtype)


def adjoint(stacked, operator):
    _, freq, receivers, sources = operator.shape
    rows = stacked.shape[1] // 2
    return pl.pallas_call(
        adjoint_kernel,
        grid=(freq,),
        in_specs=[
            pl.BlockSpec((1, 2 * rows, receivers), lambda f: (f, 0, 0)),
            pl.BlockSpec((2, 1, receivers, sources), lambda f: (0, f, 0, 0)),
        ],
        out_specs=pl.BlockSpec((2, 1, rows, sources), lambda f: (0, f, 0, 0)),
        out_shape=jax.ShapeDtypeStruct((2, freq, rows, sources), jnp.float32),
        cost_estimate=pl.CostEstimate(
            flops=8 * freq * rows * receivers * sources,
            transcendentals=0,
            bytes_accessed=operator.size * 2 + 2 * freq * rows * sources * 4,
        ),
    )(stacked, operator)


def forward_kernel(dir_ref, op_ref, out_ref):
    rows = out_ref.shape[2]
    direction = dir_ref[0]
    contract = (((1,), (1,)), ((), ()))
    by_real = lax.dot_general(direction, op_ref[0, 0], contract, preferred_element_type=jnp.float32)
    by_imag = lax.dot_general(direction, op_ref[1, 0], contract, preferred_element_type=jnp.float32)
    out_ref[0, 0] = by_real[:rows] - by_imag[rows:]
    out_ref[1, 0] = by_imag[:rows] + by_real[rows:]


def forward(stacked, operator):
    _, freq, receivers, sources = operator.shape
    rows = stacked.shape[1] // 2
    return pl.pallas_call(
        forward_kernel,
        grid=(freq,),
        in_specs=[
            pl.BlockSpec((1, 2 * rows, sources), lambda f: (f, 0, 0)),
            pl.BlockSpec((2, 1, receivers, sources), lambda f: (0, f, 0, 0)),
        ],
        out_specs=pl.BlockSpec((2, 1, rows, receivers), lambda f: (0, f, 0, 0)),
        out_shape=jax.ShapeDtypeStruct((2, freq, rows, receivers), jnp.float32),
        cost_estimate=pl.CostEstimate(
            flops=8 * freq * rows * receivers * sources,
            transcendentals=0,
            bytes_accessed=operator.size * 2 + stacked.size * 2,
        ),
    )(stacked, operator)


def on_device(operator, recorded, win_start, win_end):
    freq_local = operator.shape[1]
    sources = operator.shape[3]
    right_sides = recorded.shape[2]
    src_local = sources // lax.axis_size("recv")
    total_freq = freq_local * lax.axis_size("freq")
    columns = right_sides * src_local

    cos_part, sin_part = dft_rows(jnp.arange(total_freq, dtype=jnp.int32), total_freq)
    to_time = jnp.block([[cos_part.T, -sin_part.T], [sin_part.T, cos_part.T]])
    own_rows = lax.axis_index("freq") * freq_local + jnp.arange(freq_local, dtype=jnp.int32)
    cos_rows, sin_rows = dft_rows(own_rows, total_freq)
    to_freq = jnp.block([[cos_rows, sin_rows], [-sin_rows, cos_rows]])
    window = window_mask(
        jnp.arange(columns, dtype=jnp.int32), src_local, win_start, win_end, total_freq
    )
    window = jnp.concatenate([window, window])

    def step(iteration, state):
        reflect, residual = state
        rounded_residual = residual.astype(jnp.bfloat16)
        stacked_residual = jnp.concatenate([rounded_residual[0], rounded_residual[1]], axis=1)
        gradient = sum_scatter(
            adjoint(stacked_residual, operator).astype(jnp.bfloat16), "recv", 3
        )
        flattened = gradient.astype(jnp.bfloat16).reshape(2, freq_local, columns)
        segment = lax.all_gather(flattened, "freq", axis=1, tiled=True).astype(jnp.float32)
        timed = high_dot(to_time, segment.reshape(2 * total_freq, columns))
        projected = high_dot(to_freq, timed * window)
        direction = projected.reshape(2, freq_local, right_sides, src_local)
        rounded_direction = direction.astype(jnp.bfloat16)
        add_segment = gather_blocks(rounded_direction, "recv", 3)
        stacked_direction = jnp.concatenate([add_segment[0], add_segment[1]], axis=1)
        image = forward(stacked_direction, operator)
        sums = jnp.stack([jnp.sum(direction * direction), jnp.sum(image * image)])
        sums = jnp.sum(gather_blocks(sums[None], "recv", 0), axis=0)
        direction_power, image_energy = jnp.sum(gather_blocks(sums[None], "freq", 0), axis=0)
        step_length = direction_power / (image_energy + 1e-06)
        return (reflect + step_length * direction, residual - step_length * image)

    reflect = jnp.zeros((2, freq_local, right_sides, src_local), jnp.float32)
    return lax.fori_loop(0, ITERS, step, (reflect, recorded))


def solution(mesh):
    return jax.shard_map(
        on_device,
        mesh=mesh,
        in_specs=(
            P("groups", "freq", "recv", None),
            P("groups", "freq", None, "recv"),
            P("groups", None),
            P("groups", None),
        ),
        out_specs=(P("groups", "freq", None, "recv"), P("groups", "freq", None, "recv")),
        check_vma=False,
    )
```

```python
import math

import jax
import jax.numpy as jnp
from jax import lax
from jax.sharding import PartitionSpec as P

SBLK = 128
ITERS = 5


def high_dot(left, right):
    return jnp.dot(left, right, precision=lax.Precision.HIGH)


def dft_rows(row_ids, length):
    positions = jnp.arange(length, dtype=jnp.int32)
    phases = (row_ids[:, None] * positions[None, :] % length).astype(jnp.float32) * (
        2.0 * math.pi / length
    )
    normalizer = 1.0 / math.sqrt(length)
    return (jnp.cos(phases) * normalizer, jnp.sin(phases) * normalizer)


def window_mask(column_ids, src_local, win_start, win_end, length):
    blocks = win_start.shape[1]
    side_ids = column_ids // src_local
    source_ids = lax.axis_index("recv") * src_local + column_ids % src_local
    flat_ids = side_ids * blocks + source_ids // SBLK
    table_ids = jnp.arange(win_start.shape[0] * blocks, dtype=jnp.int32)
    matches = flat_ids[:, None] == table_ids[None, :]
    opening = jnp.sum(jnp.where(matches, win_start.reshape(-1)[None, :], 0), axis=1)
    closing = jnp.sum(jnp.where(matches, win_end.reshape(-1)[None, :], 0), axis=1)
    samples = jnp.arange(length, dtype=jnp.int32)[:, None]
    return ((samples >= opening[None, :]) & (samples < closing[None, :])).astype(jnp.float32)


def shifted(value, axis, distance):
    size = lax.axis_size(axis)
    return lax.ppermute(value, axis, [(i, (i + distance) % size) for i in range(size)])


def sum_scatter(partial, axis, dim):
    size = lax.axis_size(axis)
    me = lax.axis_index(axis)
    blocks = partial.reshape(partial.shape[:dim] + (size, partial.shape[dim] // size) + partial.shape[dim + 1 :])
    total = lax.dynamic_index_in_dim(blocks, me, axis=dim, keepdims=False).astype(jnp.float32)
    for distance in range(1, size):
        piece = lax.dynamic_index_in_dim(blocks, (me + distance) % size, axis=dim, keepdims=False)
        total = total + shifted(piece, axis, distance).astype(jnp.float32)
    return total


def gather_blocks(block, axis, dim):
    size = lax.axis_size(axis)
    me = lax.axis_index(axis)
    slots = jnp.stack([block] + [shifted(block, axis, d) for d in range(1, size)], axis=dim)
    order = (me - jnp.arange(size, dtype=jnp.int32)) % size
    ordered = jnp.take(slots, order, axis=dim)
    return ordered.reshape(block.shape[:dim] + (size * block.shape[dim],) + block.shape[dim + 1 :])


def on_device(operator, recorded, win_start, win_end):
    freq_local = operator.shape[1]
    sources = operator.shape[3]
    right_sides = recorded.shape[2]
    src_local = sources // lax.axis_size("recv")
    total_freq = freq_local * lax.axis_size("freq")
    columns = right_sides * src_local
    real_operator = operator[0]
    imag_operator = operator[1]

    cos_part, sin_part = dft_rows(jnp.arange(total_freq, dtype=jnp.int32), total_freq)
    to_time = jnp.block([[cos_part.T, -sin_part.T], [sin_part.T, cos_part.T]])
    own_rows = lax.axis_index("freq") * freq_local + jnp.arange(freq_local, dtype=jnp.int32)
    cos_rows, sin_rows = dft_rows(own_rows, total_freq)
    to_freq = jnp.block([[cos_rows, sin_rows], [-sin_rows, cos_rows]])
    window = window_mask(
        jnp.arange(columns, dtype=jnp.int32), src_local, win_start, win_end, total_freq
    )
    window = jnp.concatenate([window, window])

    def step(iteration, state):
        reflect, residual = state
        rounded_residual = residual.astype(jnp.bfloat16)
        stacked_residual = jnp.concatenate([rounded_residual[0], rounded_residual[1]], axis=1)
        with_real = jnp.einsum(
            "fbr,frs->fbs", stacked_residual, real_operator, preferred_element_type=jnp.float32
        )
        with_imag = jnp.einsum(
            "fbr,frs->fbs", stacked_residual, imag_operator, preferred_element_type=jnp.float32
        )
        partial_real = with_real[:, :right_sides] + with_imag[:, right_sides:]
        partial_imag = with_real[:, right_sides:] - with_imag[:, :right_sides]
        gradient = sum_scatter(
            jnp.stack([partial_real, partial_imag]).astype(jnp.bfloat16), "recv", 3
        )
        flattened = gradient.astype(jnp.bfloat16).reshape(2, freq_local, columns)
        segment = lax.all_gather(flattened, "freq", axis=1, tiled=True).astype(jnp.float32)
        timed = high_dot(to_time, segment.reshape(2 * total_freq, columns))
        projected = high_dot(to_freq, timed * window)
        direction = projected.reshape(2, freq_local, right_sides, src_local)
        rounded_direction = direction.astype(jnp.bfloat16)
        add_segment = gather_blocks(rounded_direction, "recv", 3)
        stacked_direction = jnp.concatenate([add_segment[0], add_segment[1]], axis=1)
        by_real = jnp.einsum(
            "fbs,frs->fbr", stacked_direction, real_operator, preferred_element_type=jnp.float32
        )
        by_imag = jnp.einsum(
            "fbs,frs->fbr", stacked_direction, imag_operator, preferred_element_type=jnp.float32
        )
        image_real = by_real[:, :right_sides] - by_imag[:, right_sides:]
        image_imag = by_imag[:, :right_sides] + by_real[:, right_sides:]
        image = jnp.stack([image_real, image_imag])
        sums = jnp.stack([jnp.sum(direction * direction), jnp.sum(image * image)])
        sums = jnp.sum(gather_blocks(sums[None], "recv", 0), axis=0)
        direction_power, image_energy = jnp.sum(gather_blocks(sums[None], "freq", 0), axis=0)
        step_length = direction_power / (image_energy + 1e-06)
        return (reflect + step_length * direction, residual - step_length * image)

    reflect = jnp.zeros((2, freq_local, right_sides, src_local), jnp.float32)
    return lax.fori_loop(0, ITERS, step, (reflect, recorded))


def solution(mesh):
    return jax.shard_map(
        on_device,
        mesh=mesh,
        in_specs=(
            P("groups", "freq", "recv", None),
            P("groups", "freq", None, "recv"),
            P("groups", None),
            P("groups", None),
        ),
        out_specs=(P("groups", "freq", None, "recv"), P("groups", "freq", None, "recv")),
        check_vma=False,
    )
```

```python
import math

import jax
import jax.numpy as jnp
from jax import lax
from jax.sharding import PartitionSpec as P

SBLK = 128
ITERS = 5


def high_dot(left, right):
    return jnp.dot(left, right, precision=lax.Precision.HIGH)


def dft_rows(row_ids, length):
    positions = jnp.arange(length, dtype=jnp.int32)
    phases = (row_ids[:, None] * positions[None, :] % length).astype(jnp.float32) * (
        2.0 * math.pi / length
    )
    normalizer = 1.0 / math.sqrt(length)
    return (jnp.cos(phases) * normalizer, jnp.sin(phases) * normalizer)


def window_mask(column_ids, src_local, win_start, win_end, length):
    blocks = win_start.shape[1]
    side_ids = column_ids // src_local
    source_ids = lax.axis_index("recv") * src_local + column_ids % src_local
    flat_ids = side_ids * blocks + source_ids // SBLK
    table_ids = jnp.arange(win_start.shape[0] * blocks, dtype=jnp.int32)
    matches = flat_ids[:, None] == table_ids[None, :]
    opening = jnp.sum(jnp.where(matches, win_start.reshape(-1)[None, :], 0), axis=1)
    closing = jnp.sum(jnp.where(matches, win_end.reshape(-1)[None, :], 0), axis=1)
    samples = jnp.arange(length, dtype=jnp.int32)[:, None]
    return ((samples >= opening[None, :]) & (samples < closing[None, :])).astype(jnp.float32)


def shifted(value, axis, distance):
    size = lax.axis_size(axis)
    return lax.ppermute(value, axis, [(i, (i + distance) % size) for i in range(size)])


def sum_scatter(partial, axis, dim):
    size = lax.axis_size(axis)
    me = lax.axis_index(axis)
    blocks = partial.reshape(partial.shape[:dim] + (size, partial.shape[dim] // size) + partial.shape[dim + 1 :])
    total = lax.dynamic_index_in_dim(blocks, me, axis=dim, keepdims=False).astype(jnp.float32)
    for distance in range(1, size):
        piece = lax.dynamic_index_in_dim(blocks, (me + distance) % size, axis=dim, keepdims=False)
        total = total + shifted(piece, axis, distance).astype(jnp.float32)
    return total


def gather_blocks(block, axis, dim):
    size = lax.axis_size(axis)
    me = lax.axis_index(axis)
    slots = jnp.stack([block] + [shifted(block, axis, d) for d in range(1, size)], axis=dim)
    order = (me - jnp.arange(size, dtype=jnp.int32)) % size
    ordered = jnp.take(slots, order, axis=dim)
    return ordered.reshape(block.shape[:dim] + (size * block.shape[dim],) + block.shape[dim + 1 :])


def gather_pairs(block, axis, dim):
    size = lax.axis_size(axis)
    me = lax.axis_index(axis)
    partner = lax.ppermute(block, axis, [(i, i ^ 1) for i in range(size)])
    first = me % 2 == 0
    pair = jnp.concatenate(
        [jnp.where(first, block, partner), jnp.where(first, partner, block)], axis=dim
    )
    pairs = size // 2
    slots = jnp.stack([pair] + [shifted(pair, axis, 2 * d) for d in range(1, pairs)], axis=dim)
    order = (me // 2 - jnp.arange(pairs, dtype=jnp.int32)) % pairs
    ordered = jnp.take(slots, order, axis=dim)
    return ordered.reshape(block.shape[:dim] + (size * block.shape[dim],) + block.shape[dim + 1 :])


def on_device(operator, recorded, win_start, win_end):
    freq_local = operator.shape[1]
    sources = operator.shape[3]
    right_sides = recorded.shape[2]
    src_local = sources // lax.axis_size("recv")
    total_freq = freq_local * lax.axis_size("freq")
    columns = right_sides * src_local
    real_operator = operator[0]
    imag_operator = operator[1]

    cos_part, sin_part = dft_rows(jnp.arange(total_freq, dtype=jnp.int32), total_freq)
    to_time = jnp.block([[cos_part.T, -sin_part.T], [sin_part.T, cos_part.T]])
    own_rows = lax.axis_index("freq") * freq_local + jnp.arange(freq_local, dtype=jnp.int32)
    cos_rows, sin_rows = dft_rows(own_rows, total_freq)
    to_freq = jnp.block([[cos_rows, sin_rows], [-sin_rows, cos_rows]])
    window = window_mask(
        jnp.arange(columns, dtype=jnp.int32), src_local, win_start, win_end, total_freq
    )
    window = jnp.concatenate([window, window])

    def step(iteration, state):
        reflect, residual = state
        rounded_residual = residual.astype(jnp.bfloat16)
        stacked_residual = jnp.concatenate([rounded_residual[0], rounded_residual[1]], axis=1)
        with_real = jnp.einsum(
            "fbr,frs->fbs", stacked_residual, real_operator, preferred_element_type=jnp.float32
        )
        with_imag = jnp.einsum(
            "fbr,frs->fbs", stacked_residual, imag_operator, preferred_element_type=jnp.float32
        )
        partial_real = with_real[:, :right_sides] + with_imag[:, right_sides:]
        partial_imag = with_real[:, right_sides:] - with_imag[:, :right_sides]
        gradient = sum_scatter(
            jnp.stack([partial_real, partial_imag]).astype(jnp.bfloat16), "recv", 3
        )
        flattened = gradient.astype(jnp.bfloat16).reshape(2, freq_local, columns)
        segment = gather_pairs(flattened, "freq", 1).astype(jnp.float32)
        timed = high_dot(to_time, segment.reshape(2 * total_freq, columns))
        projected = high_dot(to_freq, timed * window)
        direction = projected.reshape(2, freq_local, right_sides, src_local)
        rounded_direction = direction.astype(jnp.bfloat16)
        add_segment = gather_blocks(rounded_direction, "recv", 3)
        stacked_direction = jnp.concatenate([add_segment[0], add_segment[1]], axis=1)
        by_real = jnp.einsum(
            "fbs,frs->fbr", stacked_direction, real_operator, preferred_element_type=jnp.float32
        )
        by_imag = jnp.einsum(
            "fbs,frs->fbr", stacked_direction, imag_operator, preferred_element_type=jnp.float32
        )
        image_real = by_real[:, :right_sides] - by_imag[:, right_sides:]
        image_imag = by_imag[:, :right_sides] + by_real[:, right_sides:]
        image = jnp.stack([image_real, image_imag])
        sums = jnp.stack([jnp.sum(direction * direction), jnp.sum(image * image)])
        sums = jnp.sum(gather_blocks(sums[None], "recv", 0), axis=0)
        direction_power, image_energy = jnp.sum(gather_blocks(sums[None], "freq", 0), axis=0)
        step_length = direction_power / (image_energy + 1e-06)
        return (reflect + step_length * direction, residual - step_length * image)

    reflect = jnp.zeros((2, freq_local, right_sides, src_local), jnp.float32)
    return lax.fori_loop(0, ITERS, step, (reflect, recorded))


def solution(mesh):
    return jax.shard_map(
        on_device,
        mesh=mesh,
        in_specs=(
            P("groups", "freq", "recv", None),
            P("groups", "freq", None, "recv"),
            P("groups", None),
            P("groups", None),
        ),
        out_specs=(P("groups", "freq", None, "recv"), P("groups", "freq", None, "recv")),
        check_vma=False,
    )
```

```python
import math

import jax
import jax.numpy as jnp
from jax import lax
from jax.sharding import PartitionSpec as P

SBLK = 128
ITERS = 5


def high_dot(left, right):
    return jnp.dot(left, right, precision=lax.Precision.HIGH)


def dft_rows(row_ids, length):
    positions = jnp.arange(length, dtype=jnp.int32)
    phases = (row_ids[:, None] * positions[None, :] % length).astype(jnp.float32) * (
        2.0 * math.pi / length
    )
    normalizer = 1.0 / math.sqrt(length)
    return (jnp.cos(phases) * normalizer, jnp.sin(phases) * normalizer)


def window_mask(column_ids, src_local, win_start, win_end, length):
    blocks = win_start.shape[1]
    side_ids = column_ids // src_local
    source_ids = lax.axis_index("recv") * src_local + column_ids % src_local
    flat_ids = side_ids * blocks + source_ids // SBLK
    table_ids = jnp.arange(win_start.shape[0] * blocks, dtype=jnp.int32)
    matches = flat_ids[:, None] == table_ids[None, :]
    opening = jnp.sum(jnp.where(matches, win_start.reshape(-1)[None, :], 0), axis=1)
    closing = jnp.sum(jnp.where(matches, win_end.reshape(-1)[None, :], 0), axis=1)
    samples = jnp.arange(length, dtype=jnp.int32)[:, None]
    return ((samples >= opening[None, :]) & (samples < closing[None, :])).astype(jnp.float32)


def shifted(value, axis, distance):
    size = lax.axis_size(axis)
    return lax.ppermute(value, axis, [(i, (i + distance) % size) for i in range(size)])


def sum_scatter(partial, axis, dim):
    size = lax.axis_size(axis)
    me = lax.axis_index(axis)
    blocks = partial.reshape(partial.shape[:dim] + (size, partial.shape[dim] // size) + partial.shape[dim + 1 :])
    total = lax.dynamic_index_in_dim(blocks, me, axis=dim, keepdims=False).astype(jnp.float32)
    for distance in range(1, size):
        piece = lax.dynamic_index_in_dim(blocks, (me + distance) % size, axis=dim, keepdims=False)
        total = total + shifted(piece, axis, distance).astype(jnp.float32)
    return total


def gather_blocks(block, axis, dim):
    size = lax.axis_size(axis)
    me = lax.axis_index(axis)
    slots = jnp.stack([block] + [shifted(block, axis, d) for d in range(1, size)], axis=dim)
    order = (me - jnp.arange(size, dtype=jnp.int32)) % size
    ordered = jnp.take(slots, order, axis=dim)
    return ordered.reshape(block.shape[:dim] + (size * block.shape[dim],) + block.shape[dim + 1 :])


def on_device(operator, recorded, win_start, win_end):
    freq_local = operator.shape[1]
    sources = operator.shape[3]
    right_sides = recorded.shape[2]
    src_local = sources // lax.axis_size("recv")
    total_freq = freq_local * lax.axis_size("freq")
    columns = right_sides * src_local
    recv_size = lax.axis_size("recv")
    me = lax.axis_index("recv")
    blocks = operator.reshape(operator.shape[:3] + (recv_size, src_local))
    rolled = jnp.take(blocks, (me + jnp.arange(recv_size, dtype=jnp.int32)) % recv_size, axis=3)
    real_operator = rolled[0]
    imag_operator = rolled[1]

    cos_part, sin_part = dft_rows(jnp.arange(total_freq, dtype=jnp.int32), total_freq)
    to_time = jnp.block([[cos_part.T, -sin_part.T], [sin_part.T, cos_part.T]])
    own_rows = lax.axis_index("freq") * freq_local + jnp.arange(freq_local, dtype=jnp.int32)
    cos_rows, sin_rows = dft_rows(own_rows, total_freq)
    to_freq = jnp.block([[cos_rows, sin_rows], [-sin_rows, cos_rows]])
    window = window_mask(
        jnp.arange(columns, dtype=jnp.int32), src_local, win_start, win_end, total_freq
    )
    window = jnp.concatenate([window, window])

    def step(iteration, state):
        reflect, residual = state
        rounded_residual = residual.astype(jnp.bfloat16)
        stacked_residual = jnp.concatenate([rounded_residual[0], rounded_residual[1]], axis=1)
        gradient = None
        for slot in reversed(range(recv_size)):
            with_real = jnp.einsum(
                "fbr,frs->fbs", stacked_residual, real_operator[:, :, slot],
                preferred_element_type=jnp.float32,
            )
            with_imag = jnp.einsum(
                "fbr,frs->fbs", stacked_residual, imag_operator[:, :, slot],
                preferred_element_type=jnp.float32,
            )
            piece = jnp.stack(
                [
                    with_real[:, :right_sides] + with_imag[:, right_sides:],
                    with_real[:, right_sides:] - with_imag[:, :right_sides],
                ]
            ).astype(jnp.bfloat16)
            if slot:
                piece = shifted(piece, "recv", slot)
            piece = piece.astype(jnp.float32)
            gradient = piece if gradient is None else gradient + piece
        flattened = gradient.astype(jnp.bfloat16).reshape(2, freq_local, columns)
        segment = lax.all_gather(flattened, "freq", axis=1, tiled=True).astype(jnp.float32)
        timed = high_dot(to_time, segment.reshape(2 * total_freq, columns))
        projected = high_dot(to_freq, timed * window)
        direction = projected.reshape(2, freq_local, right_sides, src_local)
        rounded_direction = direction.astype(jnp.bfloat16)
        by_real = by_imag = None
        for slot in range(recv_size):
            held = rounded_direction if slot == 0 else shifted(rounded_direction, "recv", recv_size - slot)
            stacked_direction = jnp.concatenate([held[0], held[1]], axis=1)
            real_part = jnp.einsum(
                "fbs,frs->fbr", stacked_direction, real_operator[:, :, slot],
                preferred_element_type=jnp.float32,
            )
            imag_part = jnp.einsum(
                "fbs,frs->fbr", stacked_direction, imag_operator[:, :, slot],
                preferred_element_type=jnp.float32,
            )
            by_real = real_part if by_real is None else by_real + real_part
            by_imag = imag_part if by_imag is None else by_imag + imag_part
        image_real = by_real[:, :right_sides] - by_imag[:, right_sides:]
        image_imag = by_imag[:, :right_sides] + by_real[:, right_sides:]
        image = jnp.stack([image_real, image_imag])
        sums = jnp.stack([jnp.sum(direction * direction), jnp.sum(image * image)])
        sums = jnp.sum(gather_blocks(sums[None], "recv", 0), axis=0)
        direction_power, image_energy = jnp.sum(gather_blocks(sums[None], "freq", 0), axis=0)
        step_length = direction_power / (image_energy + 1e-06)
        return (reflect + step_length * direction, residual - step_length * image)

    reflect = jnp.zeros((2, freq_local, right_sides, src_local), jnp.float32)
    return lax.fori_loop(0, ITERS, step, (reflect, recorded))


def solution(mesh):
    return jax.shard_map(
        on_device,
        mesh=mesh,
        in_specs=(
            P("groups", "freq", "recv", None),
            P("groups", "freq", None, "recv"),
            P("groups", None),
            P("groups", None),
        ),
        out_specs=(P("groups", "freq", None, "recv"), P("groups", "freq", None, "recv")),
        check_vma=False,
    )
```

```python
import math

import jax
import jax.numpy as jnp
from jax import lax
from jax.sharding import PartitionSpec as P

SBLK = 128
ITERS = 5


def high_dot(left, right):
    return jnp.dot(left, right, precision=lax.Precision.HIGH)


def dft_rows(row_ids, length):
    positions = jnp.arange(length, dtype=jnp.int32)
    phases = (row_ids[:, None] * positions[None, :] % length).astype(jnp.float32) * (
        2.0 * math.pi / length
    )
    normalizer = 1.0 / math.sqrt(length)
    return (jnp.cos(phases) * normalizer, jnp.sin(phases) * normalizer)


def window_mask(column_ids, src_local, win_start, win_end, length):
    blocks = win_start.shape[1]
    side_ids = column_ids // src_local
    source_ids = lax.axis_index("recv") * src_local + column_ids % src_local
    flat_ids = side_ids * blocks + source_ids // SBLK
    table_ids = jnp.arange(win_start.shape[0] * blocks, dtype=jnp.int32)
    matches = flat_ids[:, None] == table_ids[None, :]
    opening = jnp.sum(jnp.where(matches, win_start.reshape(-1)[None, :], 0), axis=1)
    closing = jnp.sum(jnp.where(matches, win_end.reshape(-1)[None, :], 0), axis=1)
    samples = jnp.arange(length, dtype=jnp.int32)[:, None]
    return ((samples >= opening[None, :]) & (samples < closing[None, :])).astype(jnp.float32)


def shifted(value, axis, distance):
    size = lax.axis_size(axis)
    return lax.ppermute(value, axis, [(i, (i + distance) % size) for i in range(size)])


def sum_scatter(partial, axis, dim):
    size = lax.axis_size(axis)
    me = lax.axis_index(axis)
    blocks = partial.reshape(partial.shape[:dim] + (size, partial.shape[dim] // size) + partial.shape[dim + 1 :])
    total = lax.dynamic_index_in_dim(blocks, me, axis=dim, keepdims=False).astype(jnp.float32)
    for distance in range(1, size):
        piece = lax.dynamic_index_in_dim(blocks, (me + distance) % size, axis=dim, keepdims=False)
        total = total + shifted(piece, axis, distance).astype(jnp.float32)
    return total


def gather_blocks(block, axis, dim):
    size = lax.axis_size(axis)
    me = lax.axis_index(axis)
    slots = jnp.stack([block] + [shifted(block, axis, d) for d in range(1, size)], axis=dim)
    order = (me - jnp.arange(size, dtype=jnp.int32)) % size
    ordered = jnp.take(slots, order, axis=dim)
    return ordered.reshape(block.shape[:dim] + (size * block.shape[dim],) + block.shape[dim + 1 :])


def on_device(operator, recorded, win_start, win_end):
    freq_local = operator.shape[1]
    sources = operator.shape[3]
    right_sides = recorded.shape[2]
    src_local = sources // lax.axis_size("recv")
    total_freq = freq_local * lax.axis_size("freq")
    columns = right_sides * src_local
    real_operator = operator[0]
    imag_operator = operator[1]

    cos_part, sin_part = dft_rows(jnp.arange(total_freq, dtype=jnp.int32), total_freq)
    to_time = jnp.block([[cos_part.T, -sin_part.T], [sin_part.T, cos_part.T]])
    own_rows = lax.axis_index("freq") * freq_local + jnp.arange(freq_local, dtype=jnp.int32)
    cos_rows, sin_rows = dft_rows(own_rows, total_freq)
    to_freq = jnp.block([[cos_rows, sin_rows], [-sin_rows, cos_rows]])
    window = window_mask(
        jnp.arange(columns, dtype=jnp.int32), src_local, win_start, win_end, total_freq
    )
    window = jnp.concatenate([window, window])

    def adjoint(values):
        high = lax.reduce_precision(values, exponent_bits=8, mantissa_bits=7)
        low = values - high
        stacked = jnp.concatenate(
            [high[0], high[1], low[0], low[1]], axis=1
        ).astype(jnp.bfloat16)
        with_real = jnp.einsum(
            "fbr,frs->fbs", stacked, real_operator, preferred_element_type=jnp.float32
        )
        with_imag = jnp.einsum(
            "fbr,frs->fbs", stacked, imag_operator, preferred_element_type=jnp.float32
        )
        rows = right_sides
        by_real = with_real[:, : 2 * rows] + with_real[:, 2 * rows :]
        by_imag = with_imag[:, : 2 * rows] + with_imag[:, 2 * rows :]
        return jnp.stack(
            [by_real[:, :rows] + by_imag[:, rows:], by_real[:, rows:] - by_imag[:, :rows]]
        )

    def step(iteration, state):
        reflect, residual, partial = state
        gradient = sum_scatter(partial.astype(jnp.bfloat16), "recv", 3)
        flattened = gradient.astype(jnp.bfloat16).reshape(2, freq_local, columns)
        segment = lax.all_gather(flattened, "freq", axis=1, tiled=True).astype(jnp.float32)
        timed = high_dot(to_time, segment.reshape(2 * total_freq, columns))
        projected = high_dot(to_freq, timed * window)
        direction = projected.reshape(2, freq_local, right_sides, src_local)
        rounded_direction = direction.astype(jnp.bfloat16)
        add_segment = gather_blocks(rounded_direction, "recv", 3)
        stacked_direction = jnp.concatenate([add_segment[0], add_segment[1]], axis=1)
        by_real = jnp.einsum(
            "fbs,frs->fbr", stacked_direction, real_operator, preferred_element_type=jnp.float32
        )
        by_imag = jnp.einsum(
            "fbs,frs->fbr", stacked_direction, imag_operator, preferred_element_type=jnp.float32
        )
        image_real = by_real[:, :right_sides] - by_imag[:, right_sides:]
        image_imag = by_imag[:, :right_sides] + by_real[:, right_sides:]
        image = jnp.stack([image_real, image_imag])
        sums = jnp.stack([jnp.sum(direction * direction), jnp.sum(image * image)])
        sums = jnp.sum(gather_blocks(sums[None], "recv", 0), axis=0)
        direction_power, image_energy = jnp.sum(gather_blocks(sums[None], "freq", 0), axis=0)
        normal = adjoint(image)
        step_length = direction_power / (image_energy + 1e-06)
        return (
            reflect + step_length * direction,
            residual - step_length * image,
            partial - step_length * normal,
        )

    reflect = jnp.zeros((2, freq_local, right_sides, src_local), jnp.float32)
    reflect, residual, _ = lax.fori_loop(0, ITERS, step, (reflect, recorded, adjoint(recorded)))
    return (reflect, residual)


def solution(mesh):
    return jax.shard_map(
        on_device,
        mesh=mesh,
        in_specs=(
            P("groups", "freq", "recv", None),
            P("groups", "freq", None, "recv"),
            P("groups", None),
            P("groups", None),
        ),
        out_specs=(P("groups", "freq", None, "recv"), P("groups", "freq", None, "recv")),
        check_vma=False,
    )
```

```python
import math

import jax
import jax.numpy as jnp
from jax import lax
from jax.sharding import PartitionSpec as P

SBLK = 128
ITERS = 5


def high_dot(left, right):
    return jnp.dot(left, right, precision=lax.Precision.HIGH)


def dft_rows(row_ids, length):
    positions = jnp.arange(length, dtype=jnp.int32)
    phases = (row_ids[:, None] * positions[None, :] % length).astype(jnp.float32) * (
        2.0 * math.pi / length
    )
    normalizer = 1.0 / math.sqrt(length)
    return (jnp.cos(phases) * normalizer, jnp.sin(phases) * normalizer)


def window_mask(column_ids, src_local, win_start, win_end, length):
    blocks = win_start.shape[1]
    side_ids = column_ids // src_local
    source_ids = lax.axis_index("recv") * src_local + column_ids % src_local
    flat_ids = side_ids * blocks + source_ids // SBLK
    table_ids = jnp.arange(win_start.shape[0] * blocks, dtype=jnp.int32)
    matches = flat_ids[:, None] == table_ids[None, :]
    opening = jnp.sum(jnp.where(matches, win_start.reshape(-1)[None, :], 0), axis=1)
    closing = jnp.sum(jnp.where(matches, win_end.reshape(-1)[None, :], 0), axis=1)
    samples = jnp.arange(length, dtype=jnp.int32)[:, None]
    return ((samples >= opening[None, :]) & (samples < closing[None, :])).astype(jnp.float32)


def shifted(value, axis, distance):
    size = lax.axis_size(axis)
    return lax.ppermute(value, axis, [(i, (i + distance) % size) for i in range(size)])


def sum_scatter(partial, axis, dim):
    size = lax.axis_size(axis)
    me = lax.axis_index(axis)
    blocks = partial.reshape(partial.shape[:dim] + (size, partial.shape[dim] // size) + partial.shape[dim + 1 :])
    total = lax.dynamic_index_in_dim(blocks, me, axis=dim, keepdims=False).astype(jnp.float32)
    for distance in range(1, size):
        piece = lax.dynamic_index_in_dim(blocks, (me + distance) % size, axis=dim, keepdims=False)
        total = total + shifted(piece, axis, distance).astype(jnp.float32)
    return total


def gather_blocks(block, axis, dim):
    size = lax.axis_size(axis)
    me = lax.axis_index(axis)
    slots = jnp.stack([block] + [shifted(block, axis, d) for d in range(1, size)], axis=dim)
    order = (me - jnp.arange(size, dtype=jnp.int32)) % size
    ordered = jnp.take(slots, order, axis=dim)
    return ordered.reshape(block.shape[:dim] + (size * block.shape[dim],) + block.shape[dim + 1 :])


def on_device(operator, recorded, win_start, win_end):
    freq_local = operator.shape[1]
    sources = operator.shape[3]
    right_sides = recorded.shape[2]
    src_local = sources // lax.axis_size("recv")
    total_freq = freq_local * lax.axis_size("freq")
    columns = right_sides * src_local
    real_operator = operator[0]
    imag_operator = operator[1]

    cos_part, sin_part = dft_rows(jnp.arange(total_freq, dtype=jnp.int32), total_freq)
    to_time = jnp.block([[cos_part.T, -sin_part.T], [sin_part.T, cos_part.T]])
    time_high = lax.reduce_precision(to_time, exponent_bits=8, mantissa_bits=7)
    time_split = jnp.concatenate([time_high, to_time - time_high]).astype(jnp.bfloat16)
    own_rows = lax.axis_index("freq") * freq_local + jnp.arange(freq_local, dtype=jnp.int32)
    cos_rows, sin_rows = dft_rows(own_rows, total_freq)
    to_freq = jnp.block([[cos_rows, sin_rows], [-sin_rows, cos_rows]])
    window = window_mask(
        jnp.arange(columns, dtype=jnp.int32), src_local, win_start, win_end, total_freq
    )
    window = jnp.concatenate([window, window])

    def step(iteration, state):
        reflect, residual = state
        rounded_residual = residual.astype(jnp.bfloat16)
        stacked_residual = jnp.concatenate([rounded_residual[0], rounded_residual[1]], axis=1)
        with_real = jnp.einsum(
            "fbr,frs->fbs", stacked_residual, real_operator, preferred_element_type=jnp.float32
        )
        with_imag = jnp.einsum(
            "fbr,frs->fbs", stacked_residual, imag_operator, preferred_element_type=jnp.float32
        )
        partial_real = with_real[:, :right_sides] + with_imag[:, right_sides:]
        partial_imag = with_real[:, right_sides:] - with_imag[:, :right_sides]
        gradient = sum_scatter(
            jnp.stack([partial_real, partial_imag]).astype(jnp.bfloat16), "recv", 3
        )
        flattened = gradient.astype(jnp.bfloat16).reshape(2, freq_local, columns)
        segment = lax.all_gather(flattened, "freq", axis=1, tiled=True)
        both = jnp.dot(
            time_split, segment.reshape(2 * total_freq, columns), preferred_element_type=jnp.float32
        )
        timed = both[: 2 * total_freq] + both[2 * total_freq :]
        projected = high_dot(to_freq, timed * window)
        direction = projected.reshape(2, freq_local, right_sides, src_local)
        rounded_direction = direction.astype(jnp.bfloat16)
        add_segment = gather_blocks(rounded_direction, "recv", 3)
        stacked_direction = jnp.concatenate([add_segment[0], add_segment[1]], axis=1)
        by_real = jnp.einsum(
            "fbs,frs->fbr", stacked_direction, real_operator, preferred_element_type=jnp.float32
        )
        by_imag = jnp.einsum(
            "fbs,frs->fbr", stacked_direction, imag_operator, preferred_element_type=jnp.float32
        )
        image_real = by_real[:, :right_sides] - by_imag[:, right_sides:]
        image_imag = by_imag[:, :right_sides] + by_real[:, right_sides:]
        image = jnp.stack([image_real, image_imag])
        sums = jnp.stack([jnp.sum(direction * direction), jnp.sum(image * image)])
        sums = jnp.sum(gather_blocks(sums[None], "recv", 0), axis=0)
        direction_power, image_energy = jnp.sum(gather_blocks(sums[None], "freq", 0), axis=0)
        step_length = direction_power / (image_energy + 1e-06)
        return (reflect + step_length * direction, residual - step_length * image)

    reflect = jnp.zeros((2, freq_local, right_sides, src_local), jnp.float32)
    return lax.fori_loop(0, ITERS, step, (reflect, recorded))


def solution(mesh):
    return jax.shard_map(
        on_device,
        mesh=mesh,
        in_specs=(
            P("groups", "freq", "recv", None),
            P("groups", "freq", None, "recv"),
            P("groups", None),
            P("groups", None),
        ),
        out_specs=(P("groups", "freq", None, "recv"), P("groups", "freq", None, "recv")),
        check_vma=False,
    )
```
